256 devices in a mesh: docs: 32 (over y, x, z_hi), dims: 8 (over z_lo, core).
Axes of the slice: x: 4, y: 4, z: 8 (z_hi: 2, z_lo: 4; z = z_hi * 4 + z_lo), core: 2. Of those that a mesh axis runs over, the one named last changes fastest.
Arguments:
- queries: bfloat16 [16384, 3072], P('docs', 'dims'), may hold values from -6 to 6
- doc_vectors: bfloat16 [65536, 3072], P('docs', 'dims'), may hold values from -6 to 6
- surv_pairs: int32 [32, 144], P('docs'), may hold values from 0 to 2047
- surv_count: int32 [32], P('docs'), may hold values from 36 to 144, as said below
- short_pairs: int32 [32, 96], P('docs'), may hold values from 0 to 2047
- short_count: int32 [32], P('docs'), may hold values from 24 to 96, as said below
Outputs:
- prefix_scores: float32 [32, 144, 128, 128], P('docs', None, 'dims')
- full_scores: float32 [32, 96, 128, 128], P('docs', None, 'dims')
The draws below stay inside these ranges and needn't reach their ends.
Inputs may be any that keep to these rules, and one draw needn't show every extreme that they name: `surv_count`: each shard's live survivor slots; some shard has all 144 slots live. `short_count`: each shard's live shortlist slots; some shard has all 96 slots live.
All inputs are finite; a program needn't handle non-finite values.
Results may differ from the reference program's by a relative error of at most 0.0003.
Values may be sent and summed in bfloat16 or wider, within the bound.
No kernel may reach another device: no remote copies, remote signals or barrier semaphores. Data moves between devices by JAX's collectives and lax.ppermute only.
A program may use at most 128 MiB of HBM per device.

```python
import jax
import jax.numpy as jnp
from jax import lax

D = 3072
PREFIX = 768
QB = 128
DB = 128
SCAP = 144
CAP = 96
SLICE = 384
QUERIES = 16384
QBLK = 128
DOCS = 65536
DBLK_DEV = 16
N_DOCS = 32
N_DIMS = 8


def live_counts(key, capacity):
    counts = jax.random.randint(jax.random.fold_in(key, 1), (N_DOCS,), capacity // 4, capacity + 1)
    full_at = jax.random.randint(jax.random.fold_in(key, 2), (), 0, N_DOCS)
    return jnp.where(jnp.arange(N_DOCS) == full_at, capacity, counts).astype(jnp.int32)


def draw_surv_count(key, part):
    return live_counts(jax.random.fold_in(key, 11), SCAP)


def draw_short_count(key, part):
    return live_counts(jax.random.fold_in(key, 23), CAP)


def with_ends(entries, key, low, high):
    place = [jax.random.randint(jax.random.fold_in(key, axis), (), 0, length) for axis, length in enumerate(entries.shape)]
    widest = entries.shape.index(max(entries.shape))
    beside = place[:widest] + [(place[widest] + 1) % entries.shape[widest]] + place[widest + 1:]
    return entries.at[tuple(place)].set(low).at[tuple(beside)].set(high)


def steps_of(stream_key, shape, cuts, smallest, high):
    level = 1.0
    for dim, shards_of in cuts:
        draws = jax.random.uniform(jax.random.fold_in(jax.random.fold_in(stream_key, 6), dim), (shards_of,), jnp.float32, smallest / len(cuts), high / len(cuts))
        level = level * jnp.repeat(jnp.exp(draws), shape[dim] // shards_of).reshape((-1,) + (1,) * (len(shape) - 1 - dim))
    return level


def normal_values(rng, dims, scale, reach, cuts=(), kind=jnp.bfloat16):
    level = steps_of(rng, dims, cuts, -0.22, 0.18) if cuts else 1.0
    drawn = jax.random.normal(rng, dims, jnp.float32) * scale * level
    return jnp.minimum(jnp.maximum(drawn, -reach), reach).astype(kind)


def setup_inputs(seed: int = 0) -> dict:
    splits = jax.random.split(jax.random.key(seed), 7)
    queries = normal_values(splits[0], (QUERIES, D), 1.0, 6.0, ((0, 32), (1, 8)))
    doc_vectors = normal_values(splits[1], (DOCS, D), 1.0, 6.0, ((0, 32), (1, 8)))
    surv_pairs = with_ends(jax.random.randint(splits[2], (N_DOCS, SCAP), 0, QBLK * DBLK_DEV), jax.random.fold_in(splits[2], 1), 0, (QBLK * DBLK_DEV) - 1).astype(jnp.int32)
    surv_count = draw_surv_count(jax.random.fold_in(splits[6], 71), 0)
    short_pairs = with_ends(jax.random.randint(splits[4], (N_DOCS, CAP), 0, QBLK * DBLK_DEV), jax.random.fold_in(splits[4], 1), 0, (QBLK * DBLK_DEV) - 1).astype(jnp.int32)
    short_count = draw_short_count(jax.random.fold_in(splits[6], 71), 0)
    return dict(queries=queries, doc_vectors=doc_vectors, surv_pairs=surv_pairs, surv_count=surv_count, short_pairs=short_pairs, short_count=short_count)


def shard_scores(query_blocks, doc_blocks, pair_list, live_count, prefix_only):
    picked_queries = query_blocks[pair_list // DBLK_DEV]
    picked_docs = doc_blocks[pair_list % DBLK_DEV]
    totals = jnp.zeros((pair_list.shape[0], QB, DB), jnp.float32)
    for slice_index in range(N_DIMS):
        column_start = slice_index * SLICE
        query_part = picked_queries[:, :, column_start:column_start + SLICE].astype(jnp.float32)
        doc_part = picked_docs[:, :, column_start:column_start + SLICE].astype(jnp.float32)
        if prefix_only:
            columns = column_start + jnp.arange(SLICE)
            doc_part = jnp.where(columns[None, None, :] < PREFIX, doc_part, jnp.float32(0.0))
        partial_term = jnp.einsum("sqc,sdc->sqd", query_part, doc_part)
        totals = totals + partial_term
    factor = float(PREFIX) ** -0.5 if prefix_only else float(D) ** -0.5
    slots = jnp.arange(pair_list.shape[0])
    return jnp.where(slots[:, None, None] < live_count, totals * factor, jnp.float32(0.0))


def reference(queries, doc_vectors, surv_pairs, surv_count, short_pairs, short_count):
    query_blocks = queries.reshape(QBLK, QB, D)
    doc_shards = doc_vectors.reshape(N_DOCS, DBLK_DEV, DB, D)

    def prefix_shard(packed):
        return shard_scores(query_blocks, packed[0], packed[1], packed[2], True)

    def full_shard(packed):
        return shard_scores(query_blocks, packed[0], packed[1], packed[2], False)

    prefix_scores = lax.map(prefix_shard, (doc_shards, surv_pairs, surv_count))
    full_scores = lax.map(full_shard, (doc_shards, short_pairs, short_count))
    return (prefix_scores, full_scores)
```

```python
import jax
import jax.numpy as jnp
from jax import lax
from jax.sharding import Mesh
from jax.sharding import PartitionSpec as P

D = 3072
PREFIX = 768
QB = 128
DB = 128

DOCS_PARTS = (("y", 4), ("x", 4), ("zh", 2))
DIMS_PARTS = (("zl", 4), ("c", 2))
DOCS = tuple(name for name, _ in DOCS_PARTS)
DIMS = tuple(name for name, _ in DIMS_PARTS)


def shards(queries, doc_vectors, surv_pairs, surv_count, short_pairs, short_count):
    near = lax.all_gather(queries, "zh", axis=0, tiled=True)
    every_query = lax.all_gather(near, ("y", "x"), axis=0, tiled=True)
    slice_width = queries.shape[1]
    query_blocks = every_query.reshape(-1, QB, slice_width)
    doc_blocks = doc_vectors.reshape(-1, DB, slice_width)
    local_blocks = doc_blocks.shape[0]
    columns = lax.axis_index(DIMS) * slice_width + jnp.arange(slice_width)
    prefix_blocks = jnp.where(
        columns[None, None, :] < PREFIX, doc_blocks, jnp.zeros((), doc_blocks.dtype)
    )

    def pair_products(pair_ids, doc_side):
        picked_queries = jnp.take(query_blocks, pair_ids // local_blocks, axis=0)
        picked_docs = jnp.take(doc_side, pair_ids % local_blocks, axis=0)
        return jnp.einsum(
            "gqc,gdc->gqd", picked_queries, picked_docs, preferred_element_type=jnp.float32
        )

    full_terms = pair_products(short_pairs[0], doc_blocks)
    prefix_terms = pair_products(surv_pairs[0], prefix_blocks)
    prefix_sum, full_sum = (
        lax.psum_scatter(prefix_terms, DIMS, scatter_dimension=1, tiled=True),
        lax.psum_scatter(full_terms, DIMS, scatter_dimension=1, tiled=True),
    )

    def finish(summed, live_count, factor):
        slots = jnp.arange(summed.shape[0])
        return jnp.where(slots[:, None, None] < live_count, summed * factor, jnp.float32(0.0))

    prefix_out = finish(prefix_sum, surv_count[0], float(PREFIX) ** (-0.5))
    full_out = finish(full_sum, short_count[0], float(D) ** (-0.5))
    return (prefix_out[None], full_out[None])


def solution(mesh):
    sizes = [n for _, n in DOCS_PARTS + DIMS_PARTS]
    assert mesh.devices.size == jnp.prod(jnp.array(sizes))
    parts = Mesh(mesh.devices.reshape(sizes), DOCS + DIMS)
    placed = (
        P(DOCS, DIMS),
        P(DOCS, DIMS),
        P(DOCS, None),
        P(DOCS),
        P(DOCS, None),
        P(DOCS),
    )
    return jax.shard_map(
        shards,
        mesh=parts,
        in_specs=placed,
        out_specs=(P(DOCS, None, DIMS, None), P(DOCS, None, DIMS, None)),
        check_vma=False,
    )
```

```python
import jax
import jax.numpy as jnp
from jax import lax
from jax.sharding import Mesh
from jax.sharding import PartitionSpec as P

D = 3072
PREFIX = 768
QB = 128
DB = 128

DOCS_PARTS = (("y", 4), ("x", 4), ("zh", 2))
DIMS_PARTS = (("zl", 4), ("c", 2))
DOCS = tuple(name for name, _ in DOCS_PARTS)
DIMS = tuple(name for name, _ in DIMS_PARTS)


def spread_prefix(terms):
    n_zl, n_c = (n for _, n in DIMS_PARTS)
    slots, rows, cols = terms.shape
    split = terms.reshape(slots, n_zl, n_c, rows // (n_zl * n_c), cols)
    core = lax.axis_index("c")
    kept = jnp.take(split, core, axis=2)
    given = jnp.take(split, 1 - core, axis=2)
    summed = kept + lax.ppermute(given, DIMS, perm=[(0, 1), (1, 0)])
    chip = lax.axis_index("zl")
    out = summed[:, 0]
    for far in range(1, n_zl):
        moved = lax.ppermute(
            summed[:, far], DIMS, perm=[(c, far * n_c + c) for c in range(n_c)]
        )
        out = jnp.where(chip == far, moved, out)
    return out


def shards(queries, doc_vectors, surv_pairs, surv_count, short_pairs, short_count):
    near = lax.all_gather(queries, "zh", axis=0, tiled=True)
    every_query = lax.all_gather(near, ("y", "x"), axis=0, tiled=True)
    slice_width = queries.shape[1]
    query_blocks = every_query.reshape(-1, QB, slice_width)
    doc_blocks = doc_vectors.reshape(-1, DB, slice_width)
    local_blocks = doc_blocks.shape[0]
    columns = lax.axis_index(DIMS) * slice_width + jnp.arange(slice_width)
    prefix_blocks = jnp.where(
        columns[None, None, :] < PREFIX, doc_blocks, jnp.zeros((), doc_blocks.dtype)
    )

    def pair_products(pair_ids, doc_side):
        picked_queries = jnp.take(query_blocks, pair_ids // local_blocks, axis=0)
        picked_docs = jnp.take(doc_side, pair_ids % local_blocks, axis=0)
        return jnp.einsum(
            "gqc,gdc->gqd", picked_queries, picked_docs, preferred_element_type=jnp.float32
        )

    full_terms = pair_products(short_pairs[0], doc_blocks)
    full_sum = lax.psum_scatter(full_terms, DIMS, scatter_dimension=1, tiled=True)
    prefix_sum = spread_prefix(pair_products(surv_pairs[0], prefix_blocks))

    def finish(summed, live_count, factor):
        slots = jnp.arange(summed.shape[0])
        return jnp.where(slots[:, None, None] < live_count, summed * factor, jnp.float32(0.0))

    prefix_out = finish(prefix_sum, surv_count[0], float(PREFIX) ** (-0.5))
    full_out = finish(full_sum, short_count[0], float(D) ** (-0.5))
    return (prefix_out[None], full_out[None])


def solution(mesh):
    sizes = [n for _, n in DOCS_PARTS + DIMS_PARTS]
    assert mesh.devices.size == jnp.prod(jnp.array(sizes))
    parts = Mesh(mesh.devices.reshape(sizes), DOCS + DIMS)
    placed = (
        P(DOCS, DIMS),
        P(DOCS, DIMS),
        P(DOCS, None),
        P(DOCS),
        P(DOCS, None),
        P(DOCS),
    )
    return jax.shard_map(
        shards,
        mesh=parts,
        in_specs=placed,
        out_specs=(P(DOCS, None, DIMS, None), P(DOCS, None, DIMS, None)),
        check_vma=False,
    )
```

```python
import jax
import jax.numpy as jnp
from jax import lax
from jax.experimental import pallas as pl
from jax.experimental.pallas import tpu as pltpu
from jax.sharding import Mesh
from jax.sharding import PartitionSpec as P

D = 3072
PREFIX = 768
QB = 128
DB = 128

DOCS_PARTS = (("y", 4), ("x", 4), ("zh", 2))
DIMS_PARTS = (("zl", 4), ("c", 2))
DOCS = tuple(name for name, _ in DOCS_PARTS)
DIMS = tuple(name for name, _ in DIMS_PARTS)

GROUP = 8


def _pair_products(pairs, core, query_blocks, doc_blocks, split):
    slots = pairs.shape[0]
    n_docs, rows, width = doc_blocks.shape
    n_zl, n_c = (n for _, n in DIMS_PARTS)
    band = rows // (n_zl * n_c)

    def query_spec(g):
        return pl.BlockSpec(
            (1, rows, width), lambda i, ids, me: (ids[i * GROUP + g] // n_docs, 0, 0)
        )

    def kernel(ids, me, *refs):
        queries, docs, outs = refs[:GROUP], refs[GROUP], refs[GROUP + 1 :]
        step = pl.program_id(0)
        for g in range(GROUP):
            doc = docs[ids[step * GROUP + g] % n_docs]
            term = lax.dot_general(
                queries[g][0], doc, (((1,), (1,)), ((), ())),
                preferred_element_type=jnp.float32,
            )
            if not split:
                outs[0][g] = term
                continue
            first = me[0] == 0
            for chip in range(n_zl):
                lo = term[(2 * chip) * band : (2 * chip + 1) * band]
                hi = term[(2 * chip + 1) * band : (2 * chip + 2) * band]
                outs[0][chip, g] = jnp.where(first, lo, hi)
                outs[1][chip, g] = jnp.where(first, hi, lo)

    if split:
        part = jax.ShapeDtypeStruct((n_zl, slots, band, rows), jnp.float32)
        out_shape = (part, part)
        part_spec = pl.BlockSpec((n_zl, GROUP, band, rows), lambda i, ids, me: (0, i, 0, 0))
        out_specs = (part_spec, part_spec)
    else:
        out_shape = (jax.ShapeDtypeStruct((slots, rows, rows), jnp.float32),)
        out_specs = (pl.BlockSpec((GROUP, rows, rows), lambda i, ids, me: (i, 0, 0)),)
    grid_spec = pltpu.PrefetchScalarGridSpec(
        num_scalar_prefetch=2,
        grid=(slots // GROUP,),
        in_specs=[query_spec(g) for g in range(GROUP)]
        + [pl.BlockSpec((n_docs, rows, width), lambda i, ids, me: (0, 0, 0))],
        out_specs=out_specs,
    )
    cost = pl.CostEstimate(
        flops=2 * slots * rows * rows * width,
        transcendentals=0,
        bytes_accessed=slots * rows * width * 2 + n_docs * rows * width * 2 + slots * rows * rows * 4,
    )
    return pl.pallas_call(
        kernel,
        out_shape=out_shape,
        grid_spec=grid_spec,
        compiler_params=pltpu.CompilerParams(dimension_semantics=("arbitrary",)),
        cost_estimate=cost,
    )(pairs, core, *([query_blocks] * GROUP), doc_blocks)


def spread_prefix(kept, given):
    n_zl, n_c = (n for _, n in DIMS_PARTS)
    summed = kept + lax.ppermute(given, DIMS, perm=[(0, 1), (1, 0)])
    chip = lax.axis_index("zl")
    out = summed[0]
    for far in range(1, n_zl):
        moved = lax.ppermute(summed[far], DIMS, perm=[(c, far * n_c + c) for c in range(n_c)])
        out = jnp.where(chip == far, moved, out)
    return out


def shards(queries, doc_vectors, surv_pairs, surv_count, short_pairs, short_count):
    near = lax.all_gather(queries, "zh", axis=0, tiled=True)
    every_query = lax.all_gather(near, ("y", "x"), axis=0, tiled=True)
    slice_width = queries.shape[1]
    query_blocks = every_query.reshape(-1, QB, slice_width)
    doc_blocks = doc_vectors.reshape(-1, DB, slice_width)
    columns = lax.axis_index(DIMS) * slice_width + jnp.arange(slice_width)
    prefix_blocks = jnp.where(
        columns[None, None, :] < PREFIX, doc_blocks, jnp.zeros((), doc_blocks.dtype)
    )

    core = lax.axis_index("c").astype(jnp.int32).reshape(1)
    (full_terms,) = _pair_products(short_pairs[0], core, query_blocks, doc_blocks, False)
    full_sum = lax.psum_scatter(full_terms, DIMS, scatter_dimension=1, tiled=True)
    kept, given = _pair_products(surv_pairs[0], core, query_blocks, prefix_blocks, True)
    prefix_sum = spread_prefix(kept, given)

    def finish(summed, live_count, factor):
        slots = jnp.arange(summed.shape[0])
        return jnp.where(slots[:, None, None] < live_count, summed * factor, jnp.float32(0.0))

    prefix_out = finish(prefix_sum, surv_count[0], float(PREFIX) ** (-0.5))
    full_out = finish(full_sum, short_count[0], float(D) ** (-0.5))
    return (prefix_out[None], full_out[None])


def solution(mesh):
    sizes = [n for _, n in DOCS_PARTS + DIMS_PARTS]
    assert mesh.devices.size == jnp.prod(jnp.array(sizes))
    parts = Mesh(mesh.devices.reshape(sizes), DOCS + DIMS)
    placed = (
        P(DOCS, DIMS),
        P(DOCS, DIMS),
        P(DOCS, None),
        P(DOCS),
        P(DOCS, None),
        P(DOCS),
    )
    return jax.shard_map(
        shards,
        mesh=parts,
        in_specs=placed,
        out_specs=(P(DOCS, None, DIMS, None), P(DOCS, None, DIMS, None)),
        check_vma=False,
    )
```

```python
import jax
import jax.numpy as jnp
from jax import lax
from jax.experimental import pallas as pl
from jax.experimental.pallas import tpu as pltpu
from jax.sharding import Mesh
from jax.sharding import PartitionSpec as P

D = 3072
PREFIX = 768
QB = 128
DB = 128

DOCS_PARTS = (("y", 4), ("x", 4), ("zh", 2))
DIMS_PARTS = (("zl", 4), ("c", 2))
DOCS = tuple(name for name, _ in DOCS_PARTS)
DIMS = tuple(name for name, _ in DIMS_PARTS)

GROUP = 8


def _slot_products(pairs, gathered, docs, prefix):
    slots = pairs.shape[0]
    _, per_shard, rows, width = gathered.shape
    n_docs = docs.shape[-3]
    local = per_shard - 1
    band = rows // (2 * local) if prefix else rows

    def spec(g, half):
        if prefix:
            return pl.BlockSpec(
                (1, 1, band, width),
                lambda i, ids: (
                    ids[i * GROUP + g] // n_docs // local,
                    local,
                    half * local + ids[i * GROUP + g] // n_docs % local,
                    0,
                ),
            )
        return pl.BlockSpec(
            (1, 1, rows, width),
            lambda i, ids: (ids[i * GROUP + g] // n_docs // local, ids[i * GROUP + g] // n_docs % local, 0, 0),
        )

    halves = 2 if prefix else 1
    dims = (((1,), (1,)), ((), ()))

    def kernel(ids, *refs):
        picked, doc_ref, out = refs[: GROUP * halves], refs[GROUP * halves], refs[-1]
        step = pl.program_id(0)
        for g in range(GROUP):
            d = ids[step * GROUP + g] % n_docs
            if prefix:
                term = lax.dot_general(
                    picked[2 * g][0, 0], doc_ref[0, d], dims, preferred_element_type=jnp.float32
                ) + lax.dot_general(
                    picked[2 * g + 1][0, 0], doc_ref[1, d], dims, preferred_element_type=jnp.float32
                )
            else:
                term = lax.dot_general(
                    picked[g][0, 0], doc_ref[d], dims, preferred_element_type=jnp.float32
                )
            out[g] = term

    in_specs = [spec(g, h) for g in range(GROUP) for h in range(halves)]
    in_specs.append(pl.BlockSpec(docs.shape, lambda i, ids: (0,) * docs.ndim))
    grid_spec = pltpu.PrefetchScalarGridSpec(
        num_scalar_prefetch=1,
        grid=(slots // GROUP,),
        in_specs=in_specs,
        out_specs=pl.BlockSpec((GROUP, band, DB), lambda i, ids: (i, 0, 0)),
    )
    cost = pl.CostEstimate(
        flops=2 * slots * band * DB * width * halves,
        transcendentals=0,
        bytes_accessed=slots * band * width * 2 * halves + docs.size * 2 + slots * band * DB * 4,
    )
    return pl.pallas_call(
        kernel,
        out_shape=jax.ShapeDtypeStruct((slots, band, DB), jnp.float32),
        grid_spec=grid_spec,
        compiler_params=pltpu.CompilerParams(dimension_semantics=("arbitrary",)),
        cost_estimate=cost,
    )(pairs, *([gathered] * (GROUP * halves)), docs)


def shards(queries, doc_vectors, surv_pairs, surv_count, short_pairs, short_count):
    n_zl, n_c = (n for _, n in DIMS_PARTS)
    n_dims = n_zl * n_c
    n_local, width = queries.shape
    local = n_local // QB
    band = QB // n_dims

    by_band = queries.reshape(local, n_dims, band, width).transpose(1, 0, 2, 3)
    spread = lax.all_to_all(by_band, DIMS, 0, 0, tiled=True)
    prefix_rows = spread[: PREFIX // width].reshape(-1, width)
    payload = jnp.concatenate([queries, prefix_rows], axis=0)
    near = lax.all_gather(payload, "zh", axis=0, tiled=True)
    gathered = lax.all_gather(near, ("y", "x"), axis=0, tiled=True)
    gathered = gathered.reshape(-1, local + 1, QB, width)

    doc_blocks = doc_vectors.reshape(-1, DB, width)
    chip = lax.axis_index("zl")
    own_half = doc_blocks
    for far in range(1, n_zl):
        moved = lax.ppermute(doc_blocks, DIMS, perm=[(c, far * n_c + c) for c in range(n_c)])
        own_half = jnp.where(chip == far, moved, own_half)
    other_half = lax.ppermute(
        own_half, DIMS, perm=[(z * n_c + c, z * n_c + 1 - c) for z in range(n_zl) for c in range(n_c)]
    )
    core = lax.axis_index("c")
    prefix_docs = jnp.where(
        core == 0, jnp.stack([own_half, other_half]), jnp.stack([other_half, own_half])
    )

    full_terms = _slot_products(short_pairs[0], gathered, doc_blocks, False)
    full_sum = lax.psum_scatter(full_terms, DIMS, scatter_dimension=1, tiled=True)
    prefix_sum = _slot_products(surv_pairs[0], gathered, prefix_docs, True)

    def finish(summed, live_count, factor):
        slots = jnp.arange(summed.shape[0])
        return jnp.where(slots[:, None, None] < live_count, summed * factor, jnp.float32(0.0))

    prefix_out = finish(prefix_sum, surv_count[0], float(PREFIX) ** (-0.5))
    full_out = finish(full_sum, short_count[0], float(D) ** (-0.5))
    return (prefix_out[None], full_out[None])


def solution(mesh):
    sizes = [n for _, n in DOCS_PARTS + DIMS_PARTS]
    assert mesh.devices.size == jnp.prod(jnp.array(sizes))
    parts = Mesh(mesh.devices.reshape(sizes), DOCS + DIMS)
    placed = (
        P(DOCS, DIMS),
        P(DOCS, DIMS),
        P(DOCS, None),
        P(DOCS),
        P(DOCS, None),
        P(DOCS),
    )
    return jax.shard_map(
        shards,
        mesh=parts,
        in_specs=placed,
        out_specs=(P(DOCS, None, DIMS, None), P(DOCS, None, DIMS, None)),
        check_vma=False,
    )
```

```python
import jax
import jax.numpy as jnp
from jax import lax
from jax.experimental import pallas as pl
from jax.experimental.pallas import tpu as pltpu
from jax.sharding import Mesh

from jax.sharding import PartitionSpec as P

D = 3072
PREFIX = 768
QB = 128
DB = 128

DOCS_PARTS = (("y", 4), ("x", 4), ("zh", 2))
DIMS_PARTS = (("zl", 4), ("c", 2))
DOCS = tuple(name for name, _ in DOCS_PARTS)
DIMS = tuple(name for name, _ in DIMS_PARTS)

GROUP = 8


def _slot_products(pairs, gathered, docs, prefix):
    slots = pairs.shape[0]
    _, per_shard, rows, width = gathered.shape
    n_docs = docs.shape[-3]
    local = per_shard - 1
    band = rows // (2 * local) if prefix else rows

    def spec(g, half):
        if prefix:
            return pl.BlockSpec(
                (1, 1, band, width),
                lambda i, ids: (
                    ids[i * GROUP + g] // n_docs // local,
                    local,
                    half * local + ids[i * GROUP + g] // n_docs % local,
                    0,
                ),
            )
        return pl.BlockSpec(
            (1, 1, rows, width),
            lambda i, ids: (ids[i * GROUP + g] // n_docs // local, ids[i * GROUP + g] // n_docs % local, 0, 0),
        )

    halves = 2 if prefix else 1
    dims = (((1,), (1,)), ((), ()))

    def kernel(ids, *refs):
        picked, doc_ref, out = refs[: GROUP * halves], refs[GROUP * halves], refs[-1]
        step = pl.program_id(0)
        for g in range(GROUP):
            d = ids[step * GROUP + g] % n_docs
            if prefix:
                term = lax.dot_general(
                    picked[2 * g][0, 0], doc_ref[0, d], dims, preferred_element_type=jnp.float32
                ) + lax.dot_general(
                    picked[2 * g + 1][0, 0], doc_ref[1, d], dims, preferred_element_type=jnp.float32
                )
            else:
                term = lax.dot_general(
                    picked[g][0, 0], doc_ref[d], dims, preferred_element_type=jnp.float32
                )
            out[g] = term

    in_specs = [spec(g, h) for g in range(GROUP) for h in range(halves)]
    in_specs.append(pl.BlockSpec(docs.shape, lambda i, ids: (0,) * docs.ndim))
    grid_spec = pltpu.PrefetchScalarGridSpec(
        num_scalar_prefetch=1,
        grid=(slots // GROUP,),
        in_specs=in_specs,
        out_specs=pl.BlockSpec((GROUP, band, DB), lambda i, ids: (i, 0, 0)),
    )
    cost = pl.CostEstimate(
        flops=2 * slots * band * DB * width * halves,
        transcendentals=0,
        bytes_accessed=slots * band * width * 2 * halves + docs.size * 2 + slots * band * DB * 4,
    )
    return pl.pallas_call(
        kernel,
        out_shape=jax.ShapeDtypeStruct((slots, band, DB), jnp.float32),
        grid_spec=grid_spec,
        compiler_params=pltpu.CompilerParams(dimension_semantics=("arbitrary",)),
        cost_estimate=cost,
    )(pairs, *([gathered] * (GROUP * halves)), docs)


def _shards(queries, doc_vectors, surv_pairs, surv_count, short_pairs, short_count):
    n_zl, n_c = (n for _, n in DIMS_PARTS)
    n_dims = n_zl * n_c
    n_local, width = queries.shape
    local = n_local // QB
    band = QB // n_dims

    doc_blocks = doc_vectors.reshape(-1, DB, width)
    chip = lax.axis_index("zl")
    own_half = doc_blocks
    for far in range(1, n_zl):
        moved = lax.ppermute(doc_blocks, DIMS, perm=[(c, far * n_c + c) for c in range(n_c)])
        own_half = jnp.where(chip == far, moved, own_half)

    by_band = queries.reshape(local, n_dims, band, width).transpose(1, 0, 2, 3)
    spread = lax.all_to_all(by_band, DIMS, 0, 0, tiled=True)
    prefix_rows = spread[: PREFIX // width].reshape(-1, width)
    payload = jnp.concatenate([queries, prefix_rows], axis=0)
    near = lax.all_gather(payload, "zh", axis=0, tiled=True)
    gathered = lax.all_gather(near, ("y", "x"), axis=0, tiled=True)
    gathered = gathered.reshape(-1, local + 1, QB, width)

    other_half = lax.ppermute(
        own_half, DIMS, perm=[(z * n_c + c, z * n_c + 1 - c) for z in range(n_zl) for c in range(n_c)]
    )
    core = lax.axis_index("c")
    prefix_docs = jnp.where(
        core == 0, jnp.stack([own_half, other_half]), jnp.stack([other_half, own_half])
    )

    half = short_pairs.shape[1] // 2
    full_sum = jnp.concatenate(
        [
            lax.psum_scatter(
                _slot_products(ids, gathered, doc_blocks, False), DIMS, scatter_dimension=1, tiled=True
            )
            for ids in (short_pairs[0, :half], short_pairs[0, half:])
        ]
    )
    prefix_sum = _slot_products(surv_pairs[0], gathered, prefix_docs, True)

    def finish(summed, live_count, factor):
        slots = jnp.arange(summed.shape[0])
        return jnp.where(slots[:, None, None] < live_count, summed * factor, jnp.float32(0.0))

    prefix_out = finish(prefix_sum, surv_count[0], float(PREFIX) ** (-0.5))
    full_out = finish(full_sum, short_count[0], float(D) ** (-0.5))
    return (prefix_out[None], full_out[None])


def solution(mesh):
    sizes = [n for _, n in DOCS_PARTS + DIMS_PARTS]
    assert mesh.devices.size == jnp.prod(jnp.array(sizes))
    parts = Mesh(mesh.devices.reshape(sizes), DOCS + DIMS)
    placed = (
        P(DOCS, DIMS),
        P(DOCS, DIMS),
        P(DOCS, None),
        P(DOCS),
        P(DOCS, None),
        P(DOCS),
    )
    return jax.shard_map(
        _shards,
        mesh=parts,
        in_specs=placed,
        out_specs=(P(DOCS, None, DIMS, None), P(DOCS, None, DIMS, None)),
        check_vma=False,
    )
```

```python
import jax
import jax.numpy as jnp
from jax import lax
from jax.experimental import pallas as pl
from jax.experimental.pallas import tpu as pltpu
from jax.sharding import Mesh

from jax.sharding import PartitionSpec as P

D = 3072
PREFIX = 768
QB = 128
DB = 128

DOCS_PARTS = (("y", 4), ("x", 4), ("zh", 2))
DIMS_PARTS = (("zl", 4), ("c", 2))
DOCS = tuple(name for name, _ in DOCS_PARTS)
DIMS = tuple(name for name, _ in DIMS_PARTS)

GROUP = 8


def _slot_products(pairs, gathered, docs, prefix):
    slots = pairs.shape[0]
    _, per_shard, rows, width = gathered.shape
    n_docs = docs.shape[-3]
    local = per_shard - 1
    band = rows // (2 * local) if prefix else rows

    def spec(g, half):
        if prefix:
            return pl.BlockSpec(
                (1, 1, band, width),
                lambda i, ids: (
                    ids[i * GROUP + g] // n_docs // local,
                    local,
                    half * local + ids[i * GROUP + g] // n_docs % local,
                    0,
                ),
            )
        return pl.BlockSpec(
            (1, 1, rows, width),
            lambda i, ids: (ids[i * GROUP + g] // n_docs // local, ids[i * GROUP + g] // n_docs % local, 0, 0),
        )

    halves = 2 if prefix else 1
    dims = (((1,), (1,)), ((), ()))

    def kernel(ids, *refs):
        picked, doc_ref, out = refs[: GROUP * halves], refs[GROUP * halves], refs[-1]
        step = pl.program_id(0)
        for g in range(GROUP):
            d = ids[step * GROUP + g] % n_docs
            if prefix:
                term = lax.dot_general(
                    picked[2 * g][0, 0], doc_ref[0, d], dims, preferred_element_type=jnp.float32
                ) + lax.dot_general(
                    picked[2 * g + 1][0, 0], doc_ref[1, d], dims, preferred_element_type=jnp.float32
                )
            else:
                term = lax.dot_general(
                    picked[g][0, 0], doc_ref[d], dims, preferred_element_type=jnp.float32
                )
            out[g] = term

    in_specs = [spec(g, h) for g in range(GROUP) for h in range(halves)]
    in_specs.append(pl.BlockSpec(docs.shape, lambda i, ids: (0,) * docs.ndim))
    grid_spec = pltpu.PrefetchScalarGridSpec(
        num_scalar_prefetch=1,
        grid=(slots // GROUP,),
        in_specs=in_specs,
        out_specs=pl.BlockSpec((GROUP, band, DB), lambda i, ids: (i, 0, 0)),
    )
    cost = pl.CostEstimate(
        flops=2 * slots * band * DB * width * halves,
        transcendentals=0,
        bytes_accessed=slots * band * width * 2 * halves + docs.size * 2 + slots * band * DB * 4,
    )
    return pl.pallas_call(
        kernel,
        out_shape=jax.ShapeDtypeStruct((slots, band, DB), jnp.float32),
        grid_spec=grid_spec,
        compiler_params=pltpu.CompilerParams(dimension_semantics=("arbitrary",)),
        cost_estimate=cost,
    )(pairs, *([gathered] * (GROUP * halves)), docs)


def _shards(queries, doc_vectors, surv_pairs, surv_count, short_pairs, short_count):
    n_zl, n_c = (n for _, n in DIMS_PARTS)
    n_dims = n_zl * n_c
    n_local, width = queries.shape
    local = n_local // QB
    band = QB // n_dims

    doc_blocks = doc_vectors.reshape(-1, DB, width)
    chip = lax.axis_index("zl")
    own_half = doc_blocks
    for far in range(1, n_zl):
        moved = lax.ppermute(doc_blocks, DIMS, perm=[(c, far * n_c + c) for c in range(n_c)])
        own_half = jnp.where(chip == far, moved, own_half)

    by_band = queries.reshape(local, n_dims, band, width).transpose(1, 0, 2, 3)
    spread = lax.all_to_all(by_band, DIMS, 0, 0, tiled=True)
    prefix_rows = spread[: PREFIX // width].reshape(-1, width)
    near_queries = lax.all_gather(queries, "zh", axis=0, tiled=True)
    near_rows = lax.all_gather(prefix_rows, "zh", axis=0, tiled=True)
    n_zh = near_queries.shape[0] // n_local
    near = jnp.concatenate(
        [
            part.reshape(n_zh, -1, width)
            for part in (near_queries, near_rows)
        ],
        axis=1,
    ).reshape(-1, width)
    gathered = lax.all_gather(near, ("y", "x"), axis=0, tiled=True)
    gathered = gathered.reshape(-1, local + 1, QB, width)

    other_half = lax.ppermute(
        own_half, DIMS, perm=[(z * n_c + c, z * n_c + 1 - c) for z in range(n_zl) for c in range(n_c)]
    )
    core = lax.axis_index("c")
    prefix_docs = jnp.where(
        core == 0, jnp.stack([own_half, other_half]), jnp.stack([other_half, own_half])
    )

    full_terms = _slot_products(short_pairs[0], gathered, doc_blocks, False)
    full_sum = lax.psum_scatter(full_terms, DIMS, scatter_dimension=1, tiled=True)
    prefix_sum = _slot_products(surv_pairs[0], gathered, prefix_docs, True)

    def finish(summed, live_count, factor):
        slots = jnp.arange(summed.shape[0])
        return jnp.where(slots[:, None, None] < live_count, summed * factor, jnp.float32(0.0))

    prefix_out = finish(prefix_sum, surv_count[0], float(PREFIX) ** (-0.5))
    full_out = finish(full_sum, short_count[0], float(D) ** (-0.5))
    return (prefix_out[None], full_out[None])


def solution(mesh):
    sizes = [n for _, n in DOCS_PARTS + DIMS_PARTS]
    assert mesh.devices.size == jnp.prod(jnp.array(sizes))
    parts = Mesh(mesh.devices.reshape(sizes), DOCS + DIMS)
    placed = (
        P(DOCS, DIMS),
        P(DOCS, DIMS),
        P(DOCS, None),
        P(DOCS),
        P(DOCS, None),
        P(DOCS),
    )
    return jax.shard_map(
        _shards,
        mesh=parts,
        in_specs=placed,
        out_specs=(P(DOCS, None, DIMS, None), P(DOCS, None, DIMS, None)),
        check_vma=False,
    )
```

```python
import jax
import jax.numpy as jnp
from jax import lax
from jax.experimental import pallas as pl
from jax.experimental.pallas import tpu as pltpu
from jax.sharding import Mesh

from jax.sharding import PartitionSpec as P

D = 3072
PREFIX = 768
QB = 128
DB = 128

DOCS_PARTS = (("y", 4), ("x", 4), ("zh", 2))
DIMS_PARTS = (("zl", 4), ("c", 2))
DOCS = tuple(name for name, _ in DOCS_PARTS)
DIMS = tuple(name for name, _ in DIMS_PARTS)

GROUP = 16


def _slot_products(pairs, gathered, docs, prefix):
    slots = pairs.shape[0]
    _, per_shard, rows, width = gathered.shape
    n_docs = docs.shape[-3]
    local = per_shard - 1
    band = rows // (2 * local) if prefix else rows

    def spec(g, half):
        if prefix:
            return pl.BlockSpec(
                (1, 1, band, width),
                lambda i, ids: (
                    ids[i * GROUP + g] // n_docs // local,
                    local,
                    half * local + ids[i * GROUP + g] // n_docs % local,
                    0,
                ),
            )
        return pl.BlockSpec(
            (1, 1, rows, width),
            lambda i, ids: (ids[i * GROUP + g] // n_docs // local, ids[i * GROUP + g] // n_docs % local, 0, 0),
        )

    halves = 2 if prefix else 1
    dims = (((1,), (1,)), ((), ()))

    def kernel(ids, *refs):
        picked, doc_ref, out = refs[: GROUP * halves], refs[GROUP * halves], refs[-1]
        step = pl.program_id(0)
        for g in range(GROUP):
            d = ids[step * GROUP + g] % n_docs
            if prefix:
                term = lax.dot_general(
                    picked[2 * g][0, 0], doc_ref[0, d], dims, preferred_element_type=jnp.float32
                ) + lax.dot_general(
                    picked[2 * g + 1][0, 0], doc_ref[1, d], dims, preferred_element_type=jnp.float32
                )
            else:
                term = lax.dot_general(
                    picked[g][0, 0], doc_ref[d], dims, preferred_element_type=jnp.float32
                )
            out[g] = term

    in_specs = [spec(g, h) for g in range(GROUP) for h in range(halves)]
    in_specs.append(pl.BlockSpec(docs.shape, lambda i, ids: (0,) * docs.ndim))
    grid_spec = pltpu.PrefetchScalarGridSpec(
        num_scalar_prefetch=1,
        grid=(slots // GROUP,),
        in_specs=in_specs,
        out_specs=pl.BlockSpec((GROUP, band, DB), lambda i, ids: (i, 0, 0)),
    )
    cost = pl.CostEstimate(
        flops=2 * slots * band * DB * width * halves,
        transcendentals=0,
        bytes_accessed=slots * band * width * 2 * halves + docs.size * 2 + slots * band * DB * 4,
    )
    return pl.pallas_call(
        kernel,
        out_shape=jax.ShapeDtypeStruct((slots, band, DB), jnp.float32),
        grid_spec=grid_spec,
        compiler_params=pltpu.CompilerParams(dimension_semantics=("arbitrary",)),
        cost_estimate=cost,
    )(pairs, *([gathered] * (GROUP * halves)), docs)


def _shards(queries, doc_vectors, surv_pairs, surv_count, short_pairs, short_count):
    n_zl, n_c = (n for _, n in DIMS_PARTS)
    n_dims = n_zl * n_c
    n_local, width = queries.shape
    local = n_local // QB
    band = QB // n_dims

    doc_blocks = doc_vectors.reshape(-1, DB, width)
    chip = lax.axis_index("zl")
    own_half = doc_blocks
    for far in range(1, n_zl):
        moved = lax.ppermute(doc_blocks, DIMS, perm=[(c, far * n_c + c) for c in range(n_c)])
        own_half = jnp.where(chip == far, moved, own_half)

    by_band = queries.reshape(local, n_dims, band, width).transpose(1, 0, 2, 3)
    spread = lax.all_to_all(by_band, DIMS, 0, 0, tiled=True)
    prefix_rows = spread[: PREFIX // width].reshape(-1, width)
    payload = jnp.concatenate([queries, prefix_rows], axis=0)
    near = lax.all_gather(payload, "zh", axis=0, tiled=True)
    gathered = lax.all_gather(near, ("y", "x"), axis=0, tiled=True)
    gathered = gathered.reshape(-1, local + 1, QB, width)

    other_half = lax.ppermute(
        own_half, DIMS, perm=[(z * n_c + c, z * n_c + 1 - c) for z in range(n_zl) for c in range(n_c)]
    )
    core = lax.axis_index("c")
    prefix_docs = jnp.where(
        core == 0, jnp.stack([own_half, other_half]), jnp.stack([other_half, own_half])
    )

    full_terms = _slot_products(short_pairs[0], gathered, doc_blocks, False)
    full_sum = lax.psum_scatter(full_terms, DIMS, scatter_dimension=1, tiled=True)
    prefix_sum = _slot_products(surv_pairs[0], gathered, prefix_docs, True)

    def finish(summed, live_count, factor):
        slots = jnp.arange(summed.shape[0])
        return jnp.where(slots[:, None, None] < live_count, summed * factor, jnp.float32(0.0))

    prefix_out = finish(prefix_sum, surv_count[0], float(PREFIX) ** (-0.5))
    full_out = finish(full_sum, short_count[0], float(D) ** (-0.5))
    return (prefix_out[None], full_out[None])


def solution(mesh):
    sizes = [n for _, n in DOCS_PARTS + DIMS_PARTS]
    assert mesh.devices.size == jnp.prod(jnp.array(sizes))
    parts = Mesh(mesh.devices.reshape(sizes), DOCS + DIMS)
    placed = (
        P(DOCS, DIMS),
        P(DOCS, DIMS),
        P(DOCS, None),
        P(DOCS),
        P(DOCS, None),
        P(DOCS),
    )
    return jax.shard_map(
        _shards,
        mesh=parts,
        in_specs=placed,
        out_specs=(P(DOCS, None, DIMS, None), P(DOCS, None, DIMS, None)),
        check_vma=False,
    )
```

```python
import jax
import jax.numpy as jnp
from jax import lax
from jax.experimental import pallas as pl
from jax.experimental.pallas import tpu as pltpu
from jax.sharding import Mesh

from jax.sharding import PartitionSpec as P

D = 3072
PREFIX = 768
QB = 128
DB = 128

DOCS_PARTS = (("y", 4), ("x", 4), ("zh", 2))
DIMS_PARTS = (("zl", 4), ("c", 2))
DOCS = tuple(name for name, _ in DOCS_PARTS)
DIMS = tuple(name for name, _ in DIMS_PARTS)

GROUP = 16


def _slot_products(pairs, gathered, docs, prefix):
    slots = pairs.shape[0]
    _, per_shard, rows, width = gathered.shape
    n_docs = docs.shape[-3]
    local = per_shard - 1
    band = rows // (2 * local) if prefix else rows

    def spec(g, half):
        if prefix:
            return pl.BlockSpec(
                (1, 1, band, width),
                lambda i, ids: (
                    ids[i * GROUP + g] // n_docs // local,
                    local,
                    half * local + ids[i * GROUP + g] // n_docs % local,
                    0,
                ),
            )
        return pl.BlockSpec(
            (1, 1, rows, width),
            lambda i, ids: (ids[i * GROUP + g] // n_docs // local, ids[i * GROUP + g] // n_docs % local, 0, 0),
        )

    halves = 2 if prefix else 1
    dims = (((1,), (1,)), ((), ()))

    def kernel(ids, *refs):
        picked, doc_ref, out = refs[: GROUP * halves], refs[GROUP * halves], refs[-1]
        step = pl.program_id(0)
        for g in range(GROUP):
            d = ids[step * GROUP + g] % n_docs
            if prefix:
                term = lax.dot_general(
                    picked[2 * g][0, 0], doc_ref[0, d], dims, preferred_element_type=jnp.float32
                ) + lax.dot_general(
                    picked[2 * g + 1][0, 0], doc_ref[1, d], dims, preferred_element_type=jnp.float32
                )
            else:
                term = lax.dot_general(
                    picked[g][0, 0], doc_ref[d], dims, preferred_element_type=jnp.float32
                )
            out[g] = term

    in_specs = [spec(g, h) for g in range(GROUP) for h in range(halves)]
    in_specs.append(pl.BlockSpec(docs.shape, lambda i, ids: (0,) * docs.ndim))
    grid_spec = pltpu.PrefetchScalarGridSpec(
        num_scalar_prefetch=1,
        grid=(slots // GROUP,),
        in_specs=in_specs,
        out_specs=pl.BlockSpec((GROUP, band, DB), lambda i, ids: (i, 0, 0)),
    )
    cost = pl.CostEstimate(
        flops=2 * slots * band * DB * width * halves,
        transcendentals=0,
        bytes_accessed=slots * band * width * 2 * halves + docs.size * 2 + slots * band * DB * 4,
    )
    return pl.pallas_call(
        kernel,
        out_shape=jax.ShapeDtypeStruct((slots, band, DB), jnp.float32),
        grid_spec=grid_spec,
        compiler_params=pltpu.CompilerParams(dimension_semantics=("arbitrary",)),
        cost_estimate=cost,
    )(pairs, *([gathered] * (GROUP * halves)), docs)


def _shards(queries, doc_vectors, surv_pairs, surv_count, short_pairs, short_count):
    n_zl, n_c = (n for _, n in DIMS_PARTS)
    n_dims = n_zl * n_c
    n_local, width = queries.shape
    local = n_local // QB
    band = QB // n_dims

    doc_blocks = doc_vectors.reshape(-1, DB, width)
    chip = lax.axis_index("zl")
    own_half = doc_blocks
    for far in range(1, n_zl):
        moved = lax.ppermute(doc_blocks, DIMS, perm=[(c, far * n_c + c) for c in range(n_c)])
        own_half = jnp.where(chip == far, moved, own_half)

    by_band = queries.reshape(local, n_dims, band, width).transpose(1, 0, 2, 3)
    spread = lax.all_to_all(by_band, DIMS, 0, 0, tiled=True)
    prefix_rows = spread[: PREFIX // width].reshape(-1, width)
    payload = jnp.concatenate([queries, prefix_rows], axis=0)
    partner = lax.ppermute(payload, "zh", perm=[(0, 1), (1, 0)])
    low = lax.axis_index("zh") == 0
    near = jnp.where(
        low, jnp.concatenate([payload, partner]), jnp.concatenate([partner, payload])
    )
    gathered = lax.all_gather(near, ("y", "x"), axis=0, tiled=True)
    gathered = gathered.reshape(-1, local + 1, QB, width)

    other_half = lax.ppermute(
        own_half, DIMS, perm=[(z * n_c + c, z * n_c + 1 - c) for z in range(n_zl) for c in range(n_c)]
    )
    core = lax.axis_index("c")
    prefix_docs = jnp.where(
        core == 0, jnp.stack([own_half, other_half]), jnp.stack([other_half, own_half])
    )

    full_terms = _slot_products(short_pairs[0], gathered, doc_blocks, False)
    full_sum = lax.psum_scatter(full_terms, DIMS, scatter_dimension=1, tiled=True)
    prefix_sum = _slot_products(surv_pairs[0], gathered, prefix_docs, True)

    def finish(summed, live_count, factor):
        slots = jnp.arange(summed.shape[0])
        return jnp.where(slots[:, None, None] < live_count, summed * factor, jnp.float32(0.0))

    prefix_out = finish(prefix_sum, surv_count[0], float(PREFIX) ** (-0.5))
    full_out = finish(full_sum, short_count[0], float(D) ** (-0.5))
    return (prefix_out[None], full_out[None])


def solution(mesh):
    sizes = [n for _, n in DOCS_PARTS + DIMS_PARTS]
    assert mesh.devices.size == jnp.prod(jnp.array(sizes))
    parts = Mesh(mesh.devices.reshape(sizes), DOCS + DIMS)
    placed = (
        P(DOCS, DIMS),
        P(DOCS, DIMS),
        P(DOCS, None),
        P(DOCS),
        P(DOCS, None),
        P(DOCS),
    )
    return jax.shard_map(
        _shards,
        mesh=parts,
        in_specs=placed,
        out_specs=(P(DOCS, None, DIMS, None), P(DOCS, None, DIMS, None)),
        check_vma=False,
    )
```

```python
import jax
import jax.numpy as jnp
from jax import lax
from jax.experimental import pallas as pl
from jax.experimental.pallas import tpu as pltpu
from jax.sharding import Mesh

from jax.sharding import PartitionSpec as P

D = 3072
PREFIX = 768
QB = 128
DB = 128

DOCS_PARTS = (("y", 4), ("x", 4), ("zh", 2))
DIMS_PARTS = (("zl", 4), ("c", 2))
DOCS = tuple(name for name, _ in DOCS_PARTS)
DIMS = tuple(name for name, _ in DIMS_PARTS)

GROUP = 16


def _slot_products(pairs, gathered, docs, prefix, live=None, factor=None):
    slots = pairs.shape[0]
    _, per_shard, rows, width = gathered.shape
    n_docs = docs.shape[-3]
    local = per_shard - 1
    band = rows // (2 * local) if prefix else rows

    def spec(g, half):
        if prefix:
            return pl.BlockSpec(
                (1, 1, band, width),
                lambda i, ids, *_: (
                    ids[i * GROUP + g] // n_docs // local,
                    local,
                    half * local + ids[i * GROUP + g] // n_docs % local,
                    0,
                ),
            )
        return pl.BlockSpec(
            (1, 1, rows, width),
            lambda i, ids, *_: (ids[i * GROUP + g] // n_docs // local, ids[i * GROUP + g] // n_docs % local, 0, 0),
        )

    halves = 2 if prefix else 1
    dims = (((1,), (1,)), ((), ()))

    scalars = 1 if live is None else 2

    def kernel(ids, *refs):
        live_ref = refs[0] if live is not None else None
        refs = refs[scalars - 1 :]
        picked, doc_ref, out = refs[: GROUP * halves], refs[GROUP * halves], refs[-1]
        step = pl.program_id(0)
        for g in range(GROUP):
            d = ids[step * GROUP + g] % n_docs
            if prefix:
                term = lax.dot_general(
                    picked[2 * g][0, 0], doc_ref[0, d], dims, preferred_element_type=jnp.float32
                ) + lax.dot_general(
                    picked[2 * g + 1][0, 0], doc_ref[1, d], dims, preferred_element_type=jnp.float32
                )
            else:
                term = lax.dot_general(
                    picked[g][0, 0], doc_ref[d], dims, preferred_element_type=jnp.float32
                )
            if live is not None:
                slot = step * GROUP + g
                term = jnp.where(slot < live_ref[0], term * factor, jnp.zeros_like(term))
            out[g] = term

    in_specs = [spec(g, h) for g in range(GROUP) for h in range(halves)]
    in_specs.append(pl.BlockSpec(docs.shape, lambda i, ids, *_: (0,) * docs.ndim))
    grid_spec = pltpu.PrefetchScalarGridSpec(
        num_scalar_prefetch=scalars,
        grid=(slots // GROUP,),
        in_specs=in_specs,
        out_specs=pl.BlockSpec((GROUP, band, DB), lambda i, ids, *_: (i, 0, 0)),
    )
    cost = pl.CostEstimate(
        flops=2 * slots * band * DB * width * halves,
        transcendentals=0,
        bytes_accessed=slots * band * width * 2 * halves + docs.size * 2 + slots * band * DB * 4,
    )
    return pl.pallas_call(
        kernel,
        out_shape=jax.ShapeDtypeStruct((slots, band, DB), jnp.float32),
        grid_spec=grid_spec,
        compiler_params=pltpu.CompilerParams(dimension_semantics=("arbitrary",)),
        cost_estimate=cost,
    )(pairs, *(() if live is None else (live,)), *([gathered] * (GROUP * halves)), docs)


def _shards(queries, doc_vectors, surv_pairs, surv_count, short_pairs, short_count):
    n_zl, n_c = (n for _, n in DIMS_PARTS)
    n_dims = n_zl * n_c
    n_local, width = queries.shape
    local = n_local // QB
    band = QB // n_dims

    doc_blocks = doc_vectors.reshape(-1, DB, width)
    chip = lax.axis_index("zl")
    own_half = doc_blocks
    for far in range(1, n_zl):
        moved = lax.ppermute(doc_blocks, DIMS, perm=[(c, far * n_c + c) for c in range(n_c)])
        own_half = jnp.where(chip == far, moved, own_half)

    by_band = queries.reshape(local, n_dims, band, width).transpose(1, 0, 2, 3)
    spread = lax.all_to_all(by_band, DIMS, 0, 0, tiled=True)
    prefix_rows = spread[: PREFIX // width].reshape(-1, width)
    payload = jnp.concatenate([queries, prefix_rows], axis=0)
    near = lax.all_gather(payload, "zh", axis=0, tiled=True)
    gathered = lax.all_gather(near, ("y", "x"), axis=0, tiled=True)
    gathered = gathered.reshape(-1, local + 1, QB, width)

    other_half = lax.ppermute(
        own_half, DIMS, perm=[(z * n_c + c, z * n_c + 1 - c) for z in range(n_zl) for c in range(n_c)]
    )
    core = lax.axis_index("c")
    prefix_docs = jnp.where(
        core == 0, jnp.stack([own_half, other_half]), jnp.stack([other_half, own_half])
    )

    full_terms = _slot_products(
        short_pairs[0], gathered, doc_blocks, False, short_count, float(D) ** (-0.5)
    )
    full_out = lax.psum_scatter(full_terms, DIMS, scatter_dimension=1, tiled=True)
    prefix_sum = _slot_products(surv_pairs[0], gathered, prefix_docs, True)

    def finish(summed, live_count, factor):
        slots = jnp.arange(summed.shape[0])
        return jnp.where(slots[:, None, None] < live_count, summed * factor, jnp.float32(0.0))

    prefix_out = finish(prefix_sum, surv_count[0], float(PREFIX) ** (-0.5))
    return (prefix_out[None], full_out[None])


def solution(mesh):
    sizes = [n for _, n in DOCS_PARTS + DIMS_PARTS]
    assert mesh.devices.size == jnp.prod(jnp.array(sizes))
    parts = Mesh(mesh.devices.reshape(sizes), DOCS + DIMS)
    placed = (
        P(DOCS, DIMS),
        P(DOCS, DIMS),
        P(DOCS, None),
        P(DOCS),
        P(DOCS, None),
        P(DOCS),
    )
    return jax.shard_map(
        _shards,
        mesh=parts,
        in_specs=placed,
        out_specs=(P(DOCS, None, DIMS, None), P(DOCS, None, DIMS, None)),
        check_vma=False,
    )
```

```python
import jax
import jax.numpy as jnp
from jax import lax
from jax.experimental import pallas as pl
from jax.experimental.pallas import tpu as pltpu
from jax.sharding import Mesh

from jax.sharding import PartitionSpec as P

D = 3072
PREFIX = 768
QB = 128
DB = 128

DOCS_PARTS = (("y", 4), ("x", 4), ("zh", 2))
DIMS_PARTS = (("zl", 4), ("c", 2))
DOCS = tuple(name for name, _ in DOCS_PARTS)
DIMS = tuple(name for name, _ in DIMS_PARTS)

GROUP = 16


def _slot_products(pairs, gathered, docs, prefix, live=None, factor=None, group=GROUP):
    slots = pairs.shape[0]
    _, per_shard, rows, width = gathered.shape
    n_docs = docs.shape[-3]
    local = per_shard - 1
    band = rows // (2 * local) if prefix else rows

    def spec(g, half):
        if prefix:
            return pl.BlockSpec(
                (1, 1, band, width),
                lambda i, ids, *_: (
                    ids[i * group + g] // n_docs // local,
                    local,
                    half * local + ids[i * group + g] // n_docs % local,
                    0,
                ),
            )
        return pl.BlockSpec(
            (1, 1, rows, width),
            lambda i, ids, *_: (ids[i * group + g] // n_docs // local, ids[i * group + g] // n_docs % local, 0, 0),
        )

    halves = 2 if prefix else 1
    dims = (((1,), (1,)), ((), ()))

    scalars = 1 if live is None else 2

    def kernel(ids, *refs):
        live_ref = refs[0] if live is not None else None
        refs = refs[scalars - 1 :]
        picked, doc_ref, out = refs[: group * halves], refs[group * halves], refs[-1]
        step = pl.program_id(0)
        for g in range(group):
            d = ids[step * group + g] % n_docs
            if prefix:
                term = lax.dot_general(
                    picked[2 * g][0, 0], doc_ref[0, d], dims, preferred_element_type=jnp.float32
                ) + lax.dot_general(
                    picked[2 * g + 1][0, 0], doc_ref[1, d], dims, preferred_element_type=jnp.float32
                )
            else:
                term = lax.dot_general(
                    picked[g][0, 0], doc_ref[d], dims, preferred_element_type=jnp.float32
                )
            if live is not None:
                slot = step * group + g
                term = jnp.where(slot < live_ref[0], term * factor, jnp.zeros_like(term))
            out[g] = term

    in_specs = [spec(g, h) for g in range(group) for h in range(halves)]
    in_specs.append(pl.BlockSpec(docs.shape, lambda i, ids, *_: (0,) * docs.ndim))
    grid_spec = pltpu.PrefetchScalarGridSpec(
        num_scalar_prefetch=scalars,
        grid=(slots // group,),
        in_specs=in_specs,
        out_specs=pl.BlockSpec((group, band, DB), lambda i, ids, *_: (i, 0, 0)),
    )
    cost = pl.CostEstimate(
        flops=2 * slots * band * DB * width * halves,
        transcendentals=0,
        bytes_accessed=slots * band * width * 2 * halves + docs.size * 2 + slots * band * DB * 4,
    )
    return pl.pallas_call(
        kernel,
        out_shape=jax.ShapeDtypeStruct((slots, band, DB), jnp.float32),
        grid_spec=grid_spec,
        compiler_params=pltpu.CompilerParams(dimension_semantics=("arbitrary",)),
        cost_estimate=cost,
    )(pairs, *(() if live is None else (live,)), *([gathered] * (group * halves)), docs)


def _shards(queries, doc_vectors, surv_pairs, surv_count, short_pairs, short_count):
    n_zl, n_c = (n for _, n in DIMS_PARTS)
    n_dims = n_zl * n_c
    n_local, width = queries.shape
    local = n_local // QB
    band = QB // n_dims

    doc_blocks = doc_vectors.reshape(-1, DB, width)
    chip = lax.axis_index("zl")
    own_half = doc_blocks
    for far in range(1, n_zl):
        moved = lax.ppermute(doc_blocks, DIMS, perm=[(c, far * n_c + c) for c in range(n_c)])
        own_half = jnp.where(chip == far, moved, own_half)

    by_band = queries.reshape(local, n_dims, band, width).transpose(1, 0, 2, 3)
    spread = lax.all_to_all(by_band, DIMS, 0, 0, tiled=True)
    prefix_rows = spread[: PREFIX // width].reshape(-1, width)
    payload = jnp.concatenate([queries, prefix_rows], axis=0)
    near = lax.all_gather(payload, "zh", axis=0, tiled=True)
    gathered = lax.all_gather(near, ("y", "x"), axis=0, tiled=True)
    gathered = gathered.reshape(-1, local + 1, QB, width)

    other_half = lax.ppermute(
        own_half, DIMS, perm=[(z * n_c + c, z * n_c + 1 - c) for z in range(n_zl) for c in range(n_c)]
    )
    core = lax.axis_index("c")
    prefix_docs = jnp.where(
        core == 0, jnp.stack([own_half, other_half]), jnp.stack([other_half, own_half])
    )

    full_terms = _slot_products(
        short_pairs[0], gathered, doc_blocks, False, short_count, float(D) ** (-0.5), 2 * GROUP
    )
    full_out = lax.psum_scatter(full_terms, DIMS, scatter_dimension=1, tiled=True)
    prefix_sum = _slot_products(surv_pairs[0], gathered, prefix_docs, True)

    def finish(summed, live_count, factor):
        slots = jnp.arange(summed.shape[0])
        return jnp.where(slots[:, None, None] < live_count, summed * factor, jnp.float32(0.0))

    prefix_out = finish(prefix_sum, surv_count[0], float(PREFIX) ** (-0.5))
    return (prefix_out[None], full_out[None])


def solution(mesh):
    sizes = [n for _, n in DOCS_PARTS + DIMS_PARTS]
    assert mesh.devices.size == jnp.prod(jnp.array(sizes))
    parts = Mesh(mesh.devices.reshape(sizes), DOCS + DIMS)
    placed = (
        P(DOCS, DIMS),
        P(DOCS, DIMS),
        P(DOCS, None),
        P(DOCS),
        P(DOCS, None),
        P(DOCS),
    )
    return jax.shard_map(
        _shards,
        mesh=parts,
        in_specs=placed,
        out_specs=(P(DOCS, None, DIMS, None), P(DOCS, None, DIMS, None)),
        check_vma=False,
    )
```
